512 devices in a mesh: fsdp: 128 (over z, y, core), seq: 4 (over x).
Axes of the slice: x: 4, y: 4, z: 16, core: 2. Of those that a mesh axis runs over, the one named last changes fastest.
Arguments:
- tokens: bfloat16 [128, 512, 8192], P('fsdp', 'seq'), may hold values from -6 to 6
- queries: bfloat16 [128, 512, 8192], P('fsdp', None, 'seq'), may hold values from -6 to 6
- key_weight: bfloat16 [8192, 1024], P('fsdp', 'seq'), may hold values from -1 to 1
- u_factor: float32 [8192, 64], P('fsdp'), may hold values from -6 to 6
- v_factor: float32 [1024, 64], replicated, may hold values from -6 to 6
Outputs:
- update: float32 [8192, 1024], P('fsdp')
- losses: float32 [2], replicated
The draws below stay inside these ranges and needn't reach their ends.
All inputs are finite; a program needn't handle non-finite values.
Results may differ from the reference program's by a relative error of at most 0.0003.
Values may be sent and summed in bfloat16 or wider, within the bound.
No kernel may reach another device: no remote copies, remote signals or barrier semaphores. Data moves between devices by JAX's collectives and lax.ppermute only.
A program may use at most 64 MiB of HBM per device.

```python
import math
import jax
import jax.numpy as jnp
from jax import lax

D = 8192
HQ = 64
KVH = 8
HD = 128
R = 64
KD = 1024
GROUP = 8
LENGTH = 512
SEQS = 128


def common_weight(key):
    weight_key = jax.random.fold_in(key, 101)
    values = jax.random.normal(weight_key, (D, KD), jnp.float32)
    return jnp.clip(values * (1.0 / math.sqrt(D)), -1.0, 1.0)


def sequence_scales(low, ratio):
    steps = jnp.arange(SEQS).astype(jnp.float32) / float(max(SEQS - 1, 1))
    return low * jnp.exp(steps * math.log(ratio))


def draw_key_weight(key, part):
    return common_weight(key).astype(jnp.bfloat16)


def draw_tokens(key, part):
    token_key = jax.random.fold_in(key, 303)
    values = jnp.clip(jax.random.normal(token_key, (SEQS, LENGTH, D), jnp.float32), -6.0, 6.0)
    return values.astype(jnp.bfloat16)


def draw_queries(key, part):
    query_key = jax.random.fold_in(key, 404)
    values = jax.random.normal(query_key, (SEQS, LENGTH, HQ * HD), jnp.float32)
    values = jnp.clip(values * sequence_scales(0.4, 8.0)[:, None, None], -6.0, 6.0)
    return values.astype(jnp.bfloat16)


def steps_of(rng, extent, shards, least, high):
    loudness, own = 1.0, jax.random.fold_in(rng, 6)
    for axis_at, parts in shards:
        steps = jnp.exp(jax.random.uniform(jax.random.fold_in(own, axis_at), (parts,), jnp.float32, least / len(shards), high / len(shards)))
        loudness = loudness * jnp.repeat(steps, extent[axis_at] // parts).reshape([-1 if axis == axis_at else 1 for axis in range(len(extent))])
    return loudness


def noise(key, shape, width, bound, shards=(), kind=jnp.bfloat16):
    values = jax.random.normal(key, shape, jnp.float32) * width
    if len(shards) > 0:
        values = steps_of(key, shape, shards, -0.22, 0.18) * values
    return jnp.clip(values, min=-bound, max=bound).astype(kind)


def setup_inputs(seed: int = 0) -> dict:
    seeds = jax.random.split(jax.random.key(seed), 6)
    tokens = draw_tokens(jax.random.fold_in(seeds[5], 71), 0)
    queries = draw_queries(jax.random.fold_in(seeds[5], 71), 0)
    key_weight = draw_key_weight(jax.random.fold_in(seeds[5], 71), 0)
    u_factor = noise(seeds[3], (D, R), 1.0, 6.0, ((0, 128),), jnp.float32)
    v_factor = noise(seeds[4], (KD, R), 1.0, 6.0, (), jnp.float32)
    return {"tokens": tokens, "queries": queries, "key_weight": key_weight, "u_factor": u_factor, "v_factor": v_factor}


def orthonormal(factor):
    for turn in range(2):
        gram = jnp.dot(factor.T.astype(jnp.float32), factor.astype(jnp.float32), precision=lax.Precision.HIGHEST, preferred_element_type=jnp.float32)
        lower = jnp.linalg.cholesky(gram)
        factor = lax.linalg.triangular_solve(lower, factor, left_side=False, lower=True, transpose_a=True)
    return factor

def log_partition(query_rows, keys):
    length = query_rows.shape[0]
    heads = query_rows.astype(jnp.float32).reshape(length, KVH, GROUP, HD)
    key_heads = keys.astype(jnp.float32).reshape(2, length, KVH, HD)
    scores = jnp.einsum('tkgd,npkd->nkgtp', heads, key_heads) * (1.0 / math.sqrt(HD))
    places = jnp.arange(length)
    causal = places[:, None] >= places[None, :]
    scores = jnp.where(causal, scores, -1e+30)
    top = lax.optimization_barrier(jnp.max(scores, axis=-1))
    total = lax.optimization_barrier(jnp.sum(jnp.where(causal, jnp.exp(scores - top[..., None]), 0.0), axis=-1))
    return lax.optimization_barrier(jnp.sum(top + jnp.log(total), axis=(1, 2, 3)))

def reference(tokens, queries, key_weight, u_factor, v_factor):
    q_u = orthonormal(u_factor)
    q_v = orthonormal(v_factor)
    q_low = q_u.astype(jnp.bfloat16)

    def one_sequence(pair):
        rows, query_rows = pair
        base = jnp.dot(rows.astype(jnp.float32), key_weight.astype(jnp.float32), preferred_element_type=jnp.float32)
        side = jnp.dot(rows.astype(jnp.float32), q_low.astype(jnp.float32), preferred_element_type=jnp.float32)
        offset = 2.0 * jnp.dot(side.astype(jnp.float32), q_v.T.astype(jnp.float32), precision=lax.Precision.HIGHEST, preferred_element_type=jnp.float32)
        keys = jnp.stack([base + offset, base - offset]).astype(jnp.bfloat16)
        return log_partition(query_rows, keys)
    sums = lax.optimization_barrier(jnp.sum(lax.map(one_sequence, (tokens, queries)), axis=0))
    losses = sums / (SEQS * LENGTH * HQ)
    unit = math.sqrt(D * KD / R)
    update = unit * jnp.dot(q_u.astype(jnp.float32), q_v.T.astype(jnp.float32), precision=lax.Precision.HIGHEST, preferred_element_type=jnp.float32)
    return (update, losses)
```

```python
import math

import jax
import jax.numpy as jnp
from jax import lax
from jax.sharding import PartitionSpec as P

D = 8192
HQ = 64
HD = 128
R = 64
KD = 1024
GROUP = 8


def highest(left, right):
    return jnp.dot(left, right, precision=lax.Precision.HIGHEST, preferred_element_type=jnp.float32)


def solve_rows(rows, gram):
    lower = jnp.linalg.cholesky(gram)
    return lax.linalg.triangular_solve(lower, rows, left_side=False, lower=True, transpose_a=True)


def orthonormal(factor):
    for turn in range(2):
        factor = solve_rows(factor, highest(factor.T, factor))
    return factor


def split3(values):
    hi = lax.reduce_precision(values, exponent_bits=8, mantissa_bits=7)
    rest = values - hi
    mid = lax.reduce_precision(rest, exponent_bits=8, mantissa_bits=7)
    lo = rest - mid
    return [piece.astype(jnp.bfloat16) for piece in (hi, mid, lo)]


def local(tokens, queries, key_weight, u_factor, v_factor):
    n_seq = lax.axis_size("seq")
    me_seq = lax.axis_index("seq")
    me_fsdp = lax.axis_index("fsdp")
    slice_width = key_weight.shape[1]
    rows = u_factor.shape[0]

    packed = jnp.concatenate([key_weight] + split3(u_factor), axis=1)
    whole = lax.all_gather(packed, "fsdp", axis=0, tiled=True)

    x_local = tokens[0]
    chunk = x_local.shape[0]
    chunks = [x_local]
    for shift in range(1, n_seq):
        chunks.append(lax.ppermute(x_local, "seq", [(i, (i + shift) % n_seq) for i in range(n_seq)]))

    q_v = orthonormal(v_factor)
    weight_piece = whole[:, :slice_width]
    r = u_factor.shape[1]
    u_whole = (
        whole[:, slice_width : slice_width + r].astype(jnp.float32)
        + whole[:, slice_width + r : slice_width + 2 * r].astype(jnp.float32)
    ) + whole[:, slice_width + 2 * r :].astype(jnp.float32)
    q_u = orthonormal(u_whole)
    q_low = q_u.astype(jnp.bfloat16)
    both = jnp.concatenate([weight_piece, q_low], axis=1)

    col_start = me_seq * slice_width
    v_slice = lax.dynamic_slice_in_dim(q_v, col_start, slice_width, 0)
    key_parts = []
    for part in chunks:
        prod = jnp.dot(part, both, preferred_element_type=jnp.float32)
        base = prod[:, :slice_width]
        side = prod[:, slice_width:]
        offset = 2.0 * highest(side, v_slice.T)
        key_parts.append(jnp.stack([base + offset, base - offset]).astype(jnp.bfloat16))
    keys = jnp.concatenate(key_parts, axis=1)
    length = keys.shape[1]

    block = (me_seq - jnp.arange(n_seq)) % n_seq
    key_pos = (block[:, None] * chunk + jnp.arange(chunk)[None, :]).reshape(length)

    local_kv = slice_width // HD
    query_rows = queries[0]
    query_heads = query_rows.reshape(length, local_kv, GROUP, HD).transpose(1, 2, 0, 3)
    key_heads = keys.reshape(2, length, local_kv, HD).transpose(2, 0, 1, 3)
    places = jnp.arange(length)
    causal = places[:, None] >= key_pos[None, :]
    factor_scale = 1.0 / math.sqrt(HD)

    def one_query_head(query_one, key_one):
        scores = (
            jnp.einsum("td,npd->ntp", query_one, key_one, preferred_element_type=jnp.float32)
            * factor_scale
        )
        scores = jnp.where(causal[None], scores, -1e30)
        top = jnp.max(scores, axis=-1)
        total = jnp.sum(jnp.where(causal[None], jnp.exp(scores - top[..., None]), 0.0), axis=-1)
        return jnp.sum(top + jnp.log(total), axis=1)

    def one_key_head(pair):
        group_queries, key_one = pair
        return jnp.sum(
            lax.map(lambda query_one: one_query_head(query_one, key_one), group_queries), axis=0
        )

    partial_sums = jnp.sum(lax.map(one_key_head, (query_heads, key_heads)), axis=0)
    sums = lax.psum(partial_sums, ("fsdp", "seq"))
    losses = sums / (lax.axis_size("fsdp") * length * HQ)
    unit = math.sqrt(D * KD / R)
    u_rows = lax.dynamic_slice_in_dim(q_u, me_fsdp * rows, rows, 0)
    update = unit * highest(u_rows, q_v.T)
    return (update, losses)


def solution(mesh):
    in_specs = (
        P("fsdp", "seq", None),
        P("fsdp", None, "seq"),
        P("fsdp", "seq"),
        P("fsdp", None),
        P(),
    )
    out_specs = (P("fsdp", None), P())
    return jax.shard_map(local, mesh=mesh, in_specs=in_specs, out_specs=out_specs, check_vma=False)
```

```python
import math

import jax
import jax.numpy as jnp
from jax import lax
from jax.sharding import PartitionSpec as P

D = 8192
HQ = 64
HD = 128
R = 64
KD = 1024
GROUP = 8


def highest(left, right):
    return jnp.dot(left, right, precision=lax.Precision.HIGHEST, preferred_element_type=jnp.float32)


def solve_rows(rows, gram):
    lower = jnp.linalg.cholesky(gram)
    return lax.linalg.triangular_solve(lower, rows, left_side=False, lower=True, transpose_a=True)


def orthonormal(factor):
    for turn in range(2):
        factor = solve_rows(factor, highest(factor.T, factor))
    return factor


def split3(values):
    hi = lax.reduce_precision(values, exponent_bits=8, mantissa_bits=7)
    rest = values - hi
    mid = lax.reduce_precision(rest, exponent_bits=8, mantissa_bits=7)
    lo = rest - mid
    return [piece.astype(jnp.bfloat16) for piece in (hi, mid, lo)]


def total_over(values, axis):
    n = lax.axis_size(axis)
    spread = jnp.broadcast_to(values[None], (n,) + values.shape)
    return jnp.sum(lax.all_to_all(spread, axis, 0, 0, tiled=True), axis=0)


def local(tokens, queries, key_weight, u_factor, v_factor):
    n_seq = lax.axis_size("seq")
    me_seq = lax.axis_index("seq")
    me_fsdp = lax.axis_index("fsdp")
    slice_width = key_weight.shape[1]
    rows = u_factor.shape[0]

    packed = jnp.concatenate([key_weight] + split3(u_factor), axis=1)
    whole = lax.all_gather(packed, "fsdp", axis=0, tiled=True)

    x_local = tokens[0]
    chunk = x_local.shape[0]
    chunks = [x_local]
    for shift in range(1, n_seq):
        chunks.append(lax.ppermute(x_local, "seq", [(i, (i + shift) % n_seq) for i in range(n_seq)]))

    q_v = orthonormal(v_factor)
    weight_piece = whole[:, :slice_width]
    r = u_factor.shape[1]
    u_whole = (
        whole[:, slice_width : slice_width + r].astype(jnp.float32)
        + whole[:, slice_width + r : slice_width + 2 * r].astype(jnp.float32)
    ) + whole[:, slice_width + 2 * r :].astype(jnp.float32)
    q_u = orthonormal(lax.optimization_barrier(u_whole))
    q_low = q_u.astype(jnp.bfloat16)
    both = jnp.concatenate([weight_piece, q_low], axis=1)

    col_start = me_seq * slice_width
    v_slice = lax.dynamic_slice_in_dim(q_v, col_start, slice_width, 0)
    key_parts = []
    for part in chunks:
        prod = jnp.dot(part, both, preferred_element_type=jnp.float32)
        base = prod[:, :slice_width]
        side = prod[:, slice_width:]
        offset = 2.0 * highest(side, v_slice.T)
        key_parts.append(jnp.stack([base + offset, base - offset]).astype(jnp.bfloat16))
    keys = jnp.concatenate(key_parts, axis=1)
    length = keys.shape[1]

    block = (me_seq - jnp.arange(n_seq)) % n_seq
    key_pos = (block[:, None] * chunk + jnp.arange(chunk)[None, :]).reshape(length)

    local_kv = slice_width // HD
    query_rows = queries[0]
    query_heads = query_rows.reshape(length, local_kv, GROUP, HD).transpose(1, 2, 0, 3)
    key_heads = keys.reshape(2, length, local_kv, HD).transpose(2, 0, 1, 3)
    places = jnp.arange(length)
    causal = places[:, None] >= key_pos[None, :]
    factor_scale = 1.0 / math.sqrt(HD)

    def one_query_head(query_one, key_one):
        scores = (
            jnp.einsum("td,npd->ntp", query_one, key_one, preferred_element_type=jnp.float32)
            * factor_scale
        )
        scores = jnp.where(causal[None], scores, -1e30)
        top = jnp.max(scores, axis=-1)
        total = jnp.sum(jnp.where(causal[None], jnp.exp(scores - top[..., None]), 0.0), axis=-1)
        return jnp.sum(top + jnp.log(total), axis=1)

    def one_key_head(pair):
        group_queries, key_one = pair
        return jnp.sum(
            lax.map(lambda query_one: one_query_head(query_one, key_one), group_queries), axis=0
        )

    partial_sums = jnp.sum(lax.map(one_key_head, (query_heads, key_heads)), axis=0)
    sums = total_over(total_over(partial_sums, "fsdp"), "seq")
    losses = sums / (lax.axis_size("fsdp") * length * HQ)
    unit = math.sqrt(D * KD / R)
    u_rows = lax.dynamic_slice_in_dim(q_u, me_fsdp * rows, rows, 0)
    update = unit * highest(u_rows, q_v.T)
    return (update, losses)


def solution(mesh):
    in_specs = (
        P("fsdp", "seq", None),
        P("fsdp", None, "seq"),
        P("fsdp", "seq"),
        P("fsdp", None),
        P(),
    )
    out_specs = (P("fsdp", None), P())
    return jax.shard_map(local, mesh=mesh, in_specs=in_specs, out_specs=out_specs, check_vma=False)
```

```python
import math

import jax
import jax.numpy as jnp
from jax import lax
from jax.sharding import PartitionSpec as P

D = 8192
HQ = 64
HD = 128
R = 64
KD = 1024
GROUP = 8


def highest(left, right):
    return jnp.dot(left, right, precision=lax.Precision.HIGHEST, preferred_element_type=jnp.float32)


def solve_rows(rows, gram):
    lower = jnp.linalg.cholesky(gram)
    return lax.linalg.triangular_solve(lower, rows, left_side=False, lower=True, transpose_a=True)


def orthonormal(factor):
    for turn in range(2):
        factor = solve_rows(factor, highest(factor.T, factor))
    return factor


def orthonormal_map(factor):
    gram = highest(factor.T, factor)
    eye = jnp.eye(gram.shape[0], dtype=gram.dtype)
    first = lax.linalg.triangular_solve(
        jnp.linalg.cholesky(gram), eye, left_side=False, lower=True, transpose_a=True
    )
    second_gram = highest(first.T, highest(gram, first))
    second = lax.linalg.triangular_solve(
        jnp.linalg.cholesky(second_gram), eye, left_side=False, lower=True, transpose_a=True
    )
    return highest(factor, highest(first, second))


def split3(values):
    hi = lax.reduce_precision(values, exponent_bits=8, mantissa_bits=7)
    rest = values - hi
    mid = lax.reduce_precision(rest, exponent_bits=8, mantissa_bits=7)
    lo = rest - mid
    return [piece.astype(jnp.bfloat16) for piece in (hi, mid, lo)]


def total_over(values, axis):
    n = lax.axis_size(axis)
    spread = jnp.broadcast_to(values[None], (n,) + values.shape)
    return jnp.sum(lax.all_to_all(spread, axis, 0, 0, tiled=True), axis=0)


def local(tokens, queries, key_weight, u_factor, v_factor):
    n_seq = lax.axis_size("seq")
    me_seq = lax.axis_index("seq")
    me_fsdp = lax.axis_index("fsdp")
    slice_width = key_weight.shape[1]
    rows = u_factor.shape[0]

    packed = jnp.concatenate([key_weight] + split3(u_factor), axis=1)
    whole = lax.all_gather(packed, "fsdp", axis=0, tiled=True)

    x_local = tokens[0]
    chunk = x_local.shape[0]
    chunks = [x_local]
    for shift in range(1, n_seq):
        chunks.append(lax.ppermute(x_local, "seq", [(i, (i + shift) % n_seq) for i in range(n_seq)]))

    q_v = orthonormal(v_factor)
    weight_piece = whole[:, :slice_width]
    r = u_factor.shape[1]
    u_whole = (
        whole[:, slice_width : slice_width + r].astype(jnp.float32)
        + whole[:, slice_width + r : slice_width + 2 * r].astype(jnp.float32)
    ) + whole[:, slice_width + 2 * r :].astype(jnp.float32)
    q_u = orthonormal_map(lax.optimization_barrier(u_whole))
    q_low = q_u.astype(jnp.bfloat16)
    both = jnp.concatenate([weight_piece, q_low], axis=1)

    col_start = me_seq * slice_width
    v_slice = lax.dynamic_slice_in_dim(q_v, col_start, slice_width, 0)
    prod = jnp.dot(jnp.concatenate(chunks, axis=0), both, preferred_element_type=jnp.float32)
    base = prod[:, :slice_width]
    side = prod[:, slice_width:]
    offset = 2.0 * highest(side, v_slice.T)
    keys = jnp.stack([base + offset, base - offset]).astype(jnp.bfloat16)
    length = keys.shape[1]

    block = (me_seq - jnp.arange(n_seq)) % n_seq
    key_pos = (block[:, None] * chunk + jnp.arange(chunk)[None, :]).reshape(length)

    local_kv = slice_width // HD
    query_rows = queries[0]
    query_heads = query_rows.reshape(length, local_kv, GROUP, HD).transpose(1, 2, 0, 3)
    key_heads = keys.reshape(2, length, local_kv, HD).transpose(2, 0, 1, 3)
    places = jnp.arange(length)
    causal = places[:, None] >= key_pos[None, :]
    factor_scale = 1.0 / math.sqrt(HD)

    def one_query_head(query_one, key_one):
        scores = (
            jnp.einsum("td,npd->ntp", query_one, key_one, preferred_element_type=jnp.float32)
            * factor_scale
        )
        scores = jnp.where(causal[None], scores, -1e30)
        top = jnp.max(scores, axis=-1)
        total = jnp.sum(jnp.where(causal[None], jnp.exp(scores - top[..., None]), 0.0), axis=-1)
        return jnp.sum(top + jnp.log(total), axis=1)

    def one_key_head(pair):
        group_queries, key_one = pair
        return jnp.sum(
            lax.map(lambda query_one: one_query_head(query_one, key_one), group_queries), axis=0
        )

    partial_sums = jnp.sum(lax.map(one_key_head, (query_heads, key_heads)), axis=0)
    sums = total_over(total_over(partial_sums, "fsdp"), "seq")
    losses = sums / (lax.axis_size("fsdp") * length * HQ)
    unit = math.sqrt(D * KD / R)
    u_rows = lax.dynamic_slice_in_dim(q_u, me_fsdp * rows, rows, 0)
    update = unit * highest(u_rows, q_v.T)
    return (update, losses)


def solution(mesh):
    in_specs = (
        P("fsdp", "seq", None),
        P("fsdp", None, "seq"),
        P("fsdp", "seq"),
        P("fsdp", None),
        P(),
    )
    out_specs = (P("fsdp", None), P())
    return jax.shard_map(local, mesh=mesh, in_specs=in_specs, out_specs=out_specs, check_vma=False)
```

```python
import math

import jax
import jax.numpy as jnp
from jax import lax
from jax.experimental import pallas as pl
from jax.sharding import PartitionSpec as P
import functools

D = 8192
HQ = 64
HD = 128
R = 64
KD = 1024
GROUP = 8


def highest(left, right):
    return jnp.dot(left, right, precision=lax.Precision.HIGHEST, preferred_element_type=jnp.float32)


def solve_rows(rows, gram):
    lower = jnp.linalg.cholesky(gram)
    return lax.linalg.triangular_solve(lower, rows, left_side=False, lower=True, transpose_a=True)


def orthonormal(factor):
    for turn in range(2):
        factor = solve_rows(factor, highest(factor.T, factor))
    return factor


def orthonormal_map(factor):
    gram = highest(factor.T, factor)
    eye = jnp.eye(gram.shape[0], dtype=gram.dtype)
    first = lax.linalg.triangular_solve(
        jnp.linalg.cholesky(gram), eye, left_side=False, lower=True, transpose_a=True
    )
    second_gram = highest(first.T, highest(gram, first))
    second = lax.linalg.triangular_solve(
        jnp.linalg.cholesky(second_gram), eye, left_side=False, lower=True, transpose_a=True
    )
    return highest(factor, highest(first, second))


def lse_kernel(q_ref, k_ref, o_ref, *, blk, n_blk, scale):
    for p in range(2):
        for qb in range(n_blk):
            q_blk = q_ref[qb * blk:(qb + 1) * blk, :]
            m = None
            l = None
            for kb in range(qb + 1):
                k_blk = k_ref[p, kb * blk:(kb + 1) * blk, :]
                s = lax.dot_general(k_blk, q_blk, (((1,), (1,)), ((), ())),
                                    preferred_element_type=jnp.float32) * scale
                if kb == qb:
                    rows = lax.broadcasted_iota(jnp.int32, s.shape, 0)
                    cols = lax.broadcasted_iota(jnp.int32, s.shape, 1)
                    s = jnp.where(rows <= cols, s, -1e30)
                top = jnp.max(s, axis=0, keepdims=True)
                if m is None:
                    m = top
                    l = jnp.sum(jnp.exp(s - m), axis=0, keepdims=True)
                else:
                    m_new = jnp.maximum(m, top)
                    l = l * jnp.exp(m - m_new) + jnp.sum(jnp.exp(s - m_new), axis=0, keepdims=True)
                    m = m_new
            o_ref[0, p:p + 1, qb * blk:(qb + 1) * blk] = m + jnp.log(l)


def lse_rows(query_rows, keys_nat, interpret=False):
    length = query_rows.shape[0]
    heads = query_rows.shape[1] // HD
    kv = keys_nat.shape[2] // HD
    blk = 128
    kern = functools.partial(lse_kernel, blk=blk, n_blk=length // blk, scale=1.0 / math.sqrt(HD))
    return pl.pallas_call(
        kern,
        grid=(kv, GROUP),
        in_specs=[
            pl.BlockSpec((length, HD), lambda k, g: (0, k * GROUP + g)),
            pl.BlockSpec((2, length, HD), lambda k, g: (0, 0, k)),
        ],
        out_specs=pl.BlockSpec((1, 2, length), lambda k, g: (k * GROUP + g, 0, 0)),
        out_shape=jax.ShapeDtypeStruct((heads, 2, length), jnp.float32),
        interpret=interpret,
    )(query_rows, keys_nat)


def split3(values):
    hi = lax.reduce_precision(values, exponent_bits=8, mantissa_bits=7)
    rest = values - hi
    mid = lax.reduce_precision(rest, exponent_bits=8, mantissa_bits=7)
    lo = rest - mid
    return [piece.astype(jnp.bfloat16) for piece in (hi, mid, lo)]


def total_over(values, axis):
    n = lax.axis_size(axis)
    spread = jnp.broadcast_to(values[None], (n,) + values.shape)
    return jnp.sum(lax.all_to_all(spread, axis, 0, 0, tiled=True), axis=0)


def local(tokens, queries, key_weight, u_factor, v_factor):
    n_seq = lax.axis_size("seq")
    me_seq = lax.axis_index("seq")
    me_fsdp = lax.axis_index("fsdp")
    slice_width = key_weight.shape[1]
    rows = u_factor.shape[0]

    packed = jnp.concatenate([key_weight] + split3(u_factor), axis=1)
    whole = lax.all_gather(packed, "fsdp", axis=0, tiled=True)

    x_local = tokens[0]
    chunk = x_local.shape[0]
    chunks = [x_local]
    for shift in range(1, n_seq):
        chunks.append(lax.ppermute(x_local, "seq", [(i, (i + shift) % n_seq) for i in range(n_seq)]))

    q_v = orthonormal(v_factor)
    weight_piece = whole[:, :slice_width]
    r = u_factor.shape[1]
    u_whole = (
        whole[:, slice_width : slice_width + r].astype(jnp.float32)
        + whole[:, slice_width + r : slice_width + 2 * r].astype(jnp.float32)
    ) + whole[:, slice_width + 2 * r :].astype(jnp.float32)
    q_u = orthonormal_map(lax.optimization_barrier(u_whole))
    q_low = q_u.astype(jnp.bfloat16)
    both = jnp.concatenate([weight_piece, q_low], axis=1)

    col_start = me_seq * slice_width
    v_slice = lax.dynamic_slice_in_dim(q_v, col_start, slice_width, 0)
    prod = jnp.dot(jnp.concatenate(chunks, axis=0), both, preferred_element_type=jnp.float32)
    base = prod[:, :slice_width]
    side = prod[:, slice_width:]
    offset = 2.0 * highest(side, v_slice.T)
    keys = jnp.stack([base + offset, base - offset]).astype(jnp.bfloat16)
    length = keys.shape[1]

    backwards = jnp.concatenate([keys[:, (n_seq - 1 - j) * chunk : (n_seq - j) * chunk] for j in range(n_seq)], axis=1)
    doubled = jnp.concatenate([backwards, backwards], axis=1)
    start = ((n_seq - 1 - me_seq) % n_seq) * chunk
    keys_nat = lax.dynamic_slice_in_dim(doubled, start, length, 1)
    partial_sums = jnp.sum(lse_rows(queries[0], keys_nat), axis=(0, 2))
    sums = total_over(total_over(partial_sums, "fsdp"), "seq")
    losses = sums / (lax.axis_size("fsdp") * length * HQ)
    unit = math.sqrt(D * KD / R)
    u_rows = lax.dynamic_slice_in_dim(q_u, me_fsdp * rows, rows, 0)
    update = unit * highest(u_rows, q_v.T)
    return (update, losses)


def solution(mesh):
    in_specs = (
        P("fsdp", "seq", None),
        P("fsdp", None, "seq"),
        P("fsdp", "seq"),
        P("fsdp", None),
        P(),
    )
    out_specs = (P("fsdp", None), P())
    return jax.shard_map(local, mesh=mesh, in_specs=in_specs, out_specs=out_specs, check_vma=False)
```

```python
import math

import jax
import jax.numpy as jnp
from jax import lax
from jax.experimental import pallas as pl
from jax.sharding import PartitionSpec as P
import functools

D = 8192
HQ = 64
HD = 128
R = 64
KD = 1024
GROUP = 8


def highest(left, right):
    return jnp.dot(left, right, precision=lax.Precision.HIGHEST, preferred_element_type=jnp.float32)


def solve_rows(rows, gram):
    lower = jnp.linalg.cholesky(gram)
    return lax.linalg.triangular_solve(lower, rows, left_side=False, lower=True, transpose_a=True)


def orthonormal(factor):
    for turn in range(2):
        factor = solve_rows(factor, highest(factor.T, factor))
    return factor


def orthonormal_map(factor):
    gram = highest(factor.T, factor)
    eye = jnp.eye(gram.shape[0], dtype=gram.dtype)
    first = lax.linalg.triangular_solve(
        jnp.linalg.cholesky(gram), eye, left_side=False, lower=True, transpose_a=True
    )
    second_gram = highest(first.T, highest(gram, first))
    second = lax.linalg.triangular_solve(
        jnp.linalg.cholesky(second_gram), eye, left_side=False, lower=True, transpose_a=True
    )
    return highest(factor, highest(first, second))


def lse_kernel(q_ref, k_ref, o_ref, *, blk, n_blk, scale):
    for p in range(2):
        for qb in range(n_blk):
            q_blk = q_ref[qb * blk:(qb + 1) * blk, :]
            m = None
            l = None
            for kb in range(qb + 1):
                k_blk = k_ref[p, kb * blk:(kb + 1) * blk, :]
                s = lax.dot_general(k_blk, q_blk, (((1,), (1,)), ((), ())),
                                    preferred_element_type=jnp.float32) * scale
                if kb == qb:
                    rows = lax.broadcasted_iota(jnp.int32, s.shape, 0)
                    cols = lax.broadcasted_iota(jnp.int32, s.shape, 1)
                    s = jnp.where(rows <= cols, s, -1e30)
                top = jnp.max(s, axis=0, keepdims=True)
                if m is None:
                    m = top
                    l = jnp.sum(jnp.exp(s - m), axis=0, keepdims=True)
                else:
                    m_new = jnp.maximum(m, top)
                    l = l * jnp.exp(m - m_new) + jnp.sum(jnp.exp(s - m_new), axis=0, keepdims=True)
                    m = m_new
            o_ref[0, p:p + 1, qb * blk:(qb + 1) * blk] = m + jnp.log(l)


def lse_rows(query_rows, keys_nat, interpret=False):
    length = query_rows.shape[0]
    heads = query_rows.shape[1] // HD
    kv = keys_nat.shape[2] // HD
    blk = 128
    kern = functools.partial(lse_kernel, blk=blk, n_blk=length // blk, scale=1.0 / math.sqrt(HD))
    return pl.pallas_call(
        kern,
        grid=(kv, GROUP),
        in_specs=[
            pl.BlockSpec((length, HD), lambda k, g: (0, k * GROUP + g)),
            pl.BlockSpec((2, length, HD), lambda k, g: (0, 0, k)),
        ],
        out_specs=pl.BlockSpec((1, 2, length), lambda k, g: (k * GROUP + g, 0, 0)),
        out_shape=jax.ShapeDtypeStruct((heads, 2, length), jnp.float32),
        interpret=interpret,
    )(query_rows, keys_nat)


def map_from_gram(gram):
    eye = jnp.eye(gram.shape[0], dtype=gram.dtype)
    first = lax.linalg.triangular_solve(
        jnp.linalg.cholesky(gram), eye, left_side=False, lower=True, transpose_a=True
    )
    second_gram = highest(first.T, highest(gram, first))
    second = lax.linalg.triangular_solve(
        jnp.linalg.cholesky(second_gram), eye, left_side=False, lower=True, transpose_a=True
    )
    return highest(first, second)


def gram_of_pieces(pieces, r):
    full = lax.dot_general(pieces, pieces, (((0,), (0,)), ((), ())), preferred_element_type=jnp.float32)
    block = lambda a, b: full[a * r : (a + 1) * r, b * r : (b + 1) * r]
    order = [(2, 2), (2, 1), (1, 2), (1, 1), (0, 2), (2, 0), (0, 1), (1, 0), (0, 0)]
    total = block(*order[0])
    for a, b in order[1:]:
        total = total + block(a, b)
    return total


def apply_to_pieces(pieces, mapping, r):
    mh, mm, ml = split3(mapping)
    zero = jnp.zeros_like(mh)
    stack = jnp.concatenate(
        [
            jnp.concatenate([mh, mm, ml], axis=1),
            jnp.concatenate([mh, mm, zero], axis=1),
            jnp.concatenate([mh, zero, zero], axis=1),
        ],
        axis=0,
    )
    out = jnp.dot(pieces, stack, preferred_element_type=jnp.float32)
    return (out[:, 2 * r :] + out[:, r : 2 * r]) + out[:, :r]


def split3(values):
    hi = lax.reduce_precision(values, exponent_bits=8, mantissa_bits=7)
    rest = values - hi
    mid = lax.reduce_precision(rest, exponent_bits=8, mantissa_bits=7)
    lo = rest - mid
    return [piece.astype(jnp.bfloat16) for piece in (hi, mid, lo)]


def total_over(values, axis):
    n = lax.axis_size(axis)
    spread = jnp.broadcast_to(values[None], (n,) + values.shape)
    return jnp.sum(lax.all_to_all(spread, axis, 0, 0, tiled=True), axis=0)


def local(tokens, queries, key_weight, u_factor, v_factor):
    n_seq = lax.axis_size("seq")
    me_seq = lax.axis_index("seq")
    me_fsdp = lax.axis_index("fsdp")
    slice_width = key_weight.shape[1]
    rows = u_factor.shape[0]

    packed = jnp.concatenate([key_weight] + split3(u_factor), axis=1)
    whole = lax.all_gather(packed, "fsdp", axis=0, tiled=True)

    x_local = tokens[0]
    chunk = x_local.shape[0]
    chunks = [x_local]
    for shift in range(1, n_seq):
        chunks.append(lax.ppermute(x_local, "seq", [(i, (i + shift) % n_seq) for i in range(n_seq)]))

    q_v = orthonormal(v_factor)
    weight_piece = whole[:, :slice_width]
    r = u_factor.shape[1]
    pieces = whole[:, slice_width:]
    q_u = apply_to_pieces(pieces, map_from_gram(gram_of_pieces(pieces, r)), r)
    q_low = q_u.astype(jnp.bfloat16)
    both = jnp.concatenate([weight_piece, q_low], axis=1)

    col_start = me_seq * slice_width
    v_slice = lax.dynamic_slice_in_dim(q_v, col_start, slice_width, 0)
    prod = jnp.dot(jnp.concatenate(chunks, axis=0), both, preferred_element_type=jnp.float32)
    base = prod[:, :slice_width]
    side = prod[:, slice_width:]
    offset = 2.0 * highest(side, v_slice.T)
    keys = jnp.stack([base + offset, base - offset]).astype(jnp.bfloat16)
    length = keys.shape[1]

    backwards = jnp.concatenate([keys[:, (n_seq - 1 - j) * chunk : (n_seq - j) * chunk] for j in range(n_seq)], axis=1)
    doubled = jnp.concatenate([backwards, backwards], axis=1)
    start = ((n_seq - 1 - me_seq) % n_seq) * chunk
    keys_nat = lax.dynamic_slice_in_dim(doubled, start, length, 1)
    partial_sums = jnp.sum(lse_rows(queries[0], keys_nat), axis=(0, 2))
    sums = total_over(total_over(partial_sums, "fsdp"), "seq")
    losses = sums / (lax.axis_size("fsdp") * length * HQ)
    unit = math.sqrt(D * KD / R)
    u_rows = lax.dynamic_slice_in_dim(q_u, me_fsdp * rows, rows, 0)
    update = unit * highest(u_rows, q_v.T)
    return (update, losses)


def solution(mesh):
    in_specs = (
        P("fsdp", "seq", None),
        P("fsdp", None, "seq"),
        P("fsdp", "seq"),
        P("fsdp", None),
        P(),
    )
    out_specs = (P("fsdp", None), P())
    return jax.shard_map(local, mesh=mesh, in_specs=in_specs, out_specs=out_specs, check_vma=False)
```

```python
import math

import jax
import jax.numpy as jnp
from jax import lax
from jax.experimental import pallas as pl
from jax.sharding import PartitionSpec as P
import functools

D = 8192
HQ = 64
HD = 128
R = 64
KD = 1024
GROUP = 8


def highest(left, right):
    return jnp.dot(left, right, precision=lax.Precision.HIGHEST, preferred_element_type=jnp.float32)


def solve_rows(rows, gram):
    lower = jnp.linalg.cholesky(gram)
    return lax.linalg.triangular_solve(lower, rows, left_side=False, lower=True, transpose_a=True)


def orthonormal(factor):
    for turn in range(2):
        factor = solve_rows(factor, highest(factor.T, factor))
    return factor


def orthonormal_map(factor):
    gram = highest(factor.T, factor)
    eye = jnp.eye(gram.shape[0], dtype=gram.dtype)
    first = lax.linalg.triangular_solve(
        jnp.linalg.cholesky(gram), eye, left_side=False, lower=True, transpose_a=True
    )
    second_gram = highest(first.T, highest(gram, first))
    second = lax.linalg.triangular_solve(
        jnp.linalg.cholesky(second_gram), eye, left_side=False, lower=True, transpose_a=True
    )
    return highest(factor, highest(first, second))


def lse_kernel(q_ref, k_ref, o_ref, *, blk, n_blk, scale):
    for p in range(2):
        for qb in range(n_blk):
            q_blk = q_ref[qb * blk:(qb + 1) * blk, :]
            m = None
            l = None
            for kb in range(qb + 1):
                k_blk = k_ref[p, kb * blk:(kb + 1) * blk, :]
                s = lax.dot_general(k_blk, q_blk, (((1,), (1,)), ((), ())),
                                    preferred_element_type=jnp.float32) * scale
                if kb == qb:
                    rows = lax.broadcasted_iota(jnp.int32, s.shape, 0)
                    cols = lax.broadcasted_iota(jnp.int32, s.shape, 1)
                    s = jnp.where(rows <= cols, s, -1e30)
                top = jnp.max(s, axis=0, keepdims=True)
                if m is None:
                    m = top
                    l = jnp.sum(jnp.exp(s - m), axis=0, keepdims=True)
                else:
                    m_new = jnp.maximum(m, top)
                    l = l * jnp.exp(m - m_new) + jnp.sum(jnp.exp(s - m_new), axis=0, keepdims=True)
                    m = m_new
            o_ref[0, p:p + 1, qb * blk:(qb + 1) * blk] = m + jnp.log(l)


def lse_rows(query_rows, keys_nat, interpret=False):
    length = query_rows.shape[0]
    heads = query_rows.shape[1] // HD
    kv = keys_nat.shape[2] // HD
    blk = 128
    kern = functools.partial(lse_kernel, blk=blk, n_blk=length // blk, scale=1.0 / math.sqrt(HD))
    return pl.pallas_call(
        kern,
        grid=(kv, GROUP),
        in_specs=[
            pl.BlockSpec((length, HD), lambda k, g: (0, k * GROUP + g)),
            pl.BlockSpec((2, length, HD), lambda k, g: (0, 0, k)),
        ],
        out_specs=pl.BlockSpec((1, 2, length), lambda k, g: (k * GROUP + g, 0, 0)),
        out_shape=jax.ShapeDtypeStruct((heads, 2, length), jnp.float32),
        interpret=interpret,
    )(query_rows, keys_nat)


def map_from_gram(gram):
    eye = jnp.eye(gram.shape[0], dtype=gram.dtype)
    first = lax.linalg.triangular_solve(
        jnp.linalg.cholesky(gram), eye, left_side=False, lower=True, transpose_a=True
    )
    second_gram = highest(first.T, highest(gram, first))
    second = lax.linalg.triangular_solve(
        jnp.linalg.cholesky(second_gram), eye, left_side=False, lower=True, transpose_a=True
    )
    return highest(first, second)


def gram_of_pieces(pieces, r):
    full = lax.dot_general(pieces, pieces, (((0,), (0,)), ((), ())), preferred_element_type=jnp.float32)
    block = lambda a, b: full[a * r : (a + 1) * r, b * r : (b + 1) * r]
    order = [(1, 1), (0, 1), (1, 0), (0, 0)]
    total = block(*order[0])
    for a, b in order[1:]:
        total = total + block(a, b)
    return total


def apply_to_pieces(pieces, mapping, r):
    mh, mm, ml = split3(mapping)
    zero = jnp.zeros_like(mh)
    stack = jnp.concatenate(
        [
            jnp.concatenate([mh, mm, ml], axis=1),
            jnp.concatenate([mh, mm, zero], axis=1),
        ],
        axis=0,
    )
    out = jnp.dot(pieces, stack, preferred_element_type=jnp.float32)
    return (out[:, 2 * r :] + out[:, r : 2 * r]) + out[:, :r]


def split3(values):
    hi = lax.reduce_precision(values, exponent_bits=8, mantissa_bits=7)
    rest = values - hi
    mid = lax.reduce_precision(rest, exponent_bits=8, mantissa_bits=7)
    lo = rest - mid
    return [piece.astype(jnp.bfloat16) for piece in (hi, mid, lo)]


def total_over(values, axis):
    n = lax.axis_size(axis)
    spread = jnp.broadcast_to(values[None], (n,) + values.shape)
    return jnp.sum(lax.all_to_all(spread, axis, 0, 0, tiled=True), axis=0)


def local(tokens, queries, key_weight, u_factor, v_factor):
    n_seq = lax.axis_size("seq")
    me_seq = lax.axis_index("seq")
    me_fsdp = lax.axis_index("fsdp")
    slice_width = key_weight.shape[1]
    rows = u_factor.shape[0]

    packed = jnp.concatenate([key_weight] + split3(u_factor)[:2], axis=1)
    whole = lax.all_gather(packed, "fsdp", axis=0, tiled=True)

    x_local = tokens[0]
    chunk = x_local.shape[0]
    chunks = [x_local]
    for shift in range(1, n_seq):
        chunks.append(lax.ppermute(x_local, "seq", [(i, (i + shift) % n_seq) for i in range(n_seq)]))

    q_v = orthonormal(v_factor)
    weight_piece = whole[:, :slice_width]
    r = u_factor.shape[1]
    pieces = whole[:, slice_width:]
    q_u = apply_to_pieces(pieces, map_from_gram(gram_of_pieces(pieces, r)), r)
    q_low = q_u.astype(jnp.bfloat16)
    both = jnp.concatenate([weight_piece, q_low], axis=1)

    col_start = me_seq * slice_width
    v_slice = lax.dynamic_slice_in_dim(q_v, col_start, slice_width, 0)
    prod = jnp.dot(jnp.concatenate(chunks, axis=0), both, preferred_element_type=jnp.float32)
    base = prod[:, :slice_width]
    side = prod[:, slice_width:]
    offset = 2.0 * highest(side, v_slice.T)
    keys = jnp.stack([base + offset, base - offset]).astype(jnp.bfloat16)
    length = keys.shape[1]

    backwards = jnp.concatenate([keys[:, (n_seq - 1 - j) * chunk : (n_seq - j) * chunk] for j in range(n_seq)], axis=1)
    doubled = jnp.concatenate([backwards, backwards], axis=1)
    start = ((n_seq - 1 - me_seq) % n_seq) * chunk
    keys_nat = lax.dynamic_slice_in_dim(doubled, start, length, 1)
    partial_sums = jnp.sum(lse_rows(queries[0], keys_nat), axis=(0, 2))
    sums = total_over(total_over(partial_sums, "fsdp"), "seq")
    losses = sums / (lax.axis_size("fsdp") * length * HQ)
    unit = math.sqrt(D * KD / R)
    u_rows = lax.dynamic_slice_in_dim(q_u, me_fsdp * rows, rows, 0)
    update = unit * highest(u_rows, q_v.T)
    return (update, losses)


def solution(mesh):
    in_specs = (
        P("fsdp", "seq", None),
        P("fsdp", None, "seq"),
        P("fsdp", "seq"),
        P("fsdp", None),
        P(),
    )
    out_specs = (P("fsdp", None), P())
    return jax.shard_map(local, mesh=mesh, in_specs=in_specs, out_specs=out_specs, check_vma=False)
```

```python
import math

import jax
import jax.numpy as jnp
from jax import lax
from jax.experimental import pallas as pl
from jax.sharding import PartitionSpec as P
import functools

D = 8192
HQ = 64
HD = 128
R = 64
KD = 1024
GROUP = 8


def highest(left, right):
    return jnp.dot(left, right, precision=lax.Precision.HIGHEST, preferred_element_type=jnp.float32)


def solve_rows(rows, gram):
    lower = jnp.linalg.cholesky(gram)
    return lax.linalg.triangular_solve(lower, rows, left_side=False, lower=True, transpose_a=True)


def orthonormal(factor):
    for turn in range(2):
        factor = solve_rows(factor, highest(factor.T, factor))
    return factor


def orthonormal_map(factor):
    gram = highest(factor.T, factor)
    eye = jnp.eye(gram.shape[0], dtype=gram.dtype)
    first = lax.linalg.triangular_solve(
        jnp.linalg.cholesky(gram), eye, left_side=False, lower=True, transpose_a=True
    )
    second_gram = highest(first.T, highest(gram, first))
    second = lax.linalg.triangular_solve(
        jnp.linalg.cholesky(second_gram), eye, left_side=False, lower=True, transpose_a=True
    )
    return highest(factor, highest(first, second))


def lse_kernel(q_ref, k_ref, o_ref, *, blk, n_blk, scale):
    def one_head(g, carry):
        col = pl.multiple_of(g * HD, HD)
        for p in range(2):
            for qb in range(n_blk):
                q_blk = q_ref[qb * blk:(qb + 1) * blk, pl.ds(col, HD)]
                m = None
                l = None
                for kb in range(qb + 1):
                    k_blk = k_ref[p, kb * blk:(kb + 1) * blk, :]
                    s = lax.dot_general(k_blk, q_blk, (((1,), (1,)), ((), ())),
                                        preferred_element_type=jnp.float32) * scale
                    if kb == qb:
                        rows = lax.broadcasted_iota(jnp.int32, s.shape, 0)
                        cols = lax.broadcasted_iota(jnp.int32, s.shape, 1)
                        s = jnp.where(rows <= cols, s, -1e30)
                    top = jnp.max(s, axis=0, keepdims=True)
                    if m is None:
                        m = top
                        l = jnp.sum(jnp.exp(s - m), axis=0, keepdims=True)
                    else:
                        m_new = jnp.maximum(m, top)
                        l = l * jnp.exp(m - m_new) + jnp.sum(jnp.exp(s - m_new), axis=0, keepdims=True)
                        m = m_new
                o_ref[pl.ds(g, 1), p, qb * blk:(qb + 1) * blk] = (m + jnp.log(l))
        return carry

    lax.fori_loop(0, GROUP, one_head, 0)


def lse_rows(query_rows, keys_nat, interpret=False):
    length = query_rows.shape[0]
    heads = query_rows.shape[1] // HD
    kv = keys_nat.shape[2] // HD
    blk = 128
    kern = functools.partial(lse_kernel, blk=blk, n_blk=length // blk, scale=1.0 / math.sqrt(HD))
    return pl.pallas_call(
        kern,
        grid=(kv,),
        in_specs=[
            pl.BlockSpec((length, GROUP * HD), lambda k: (0, k)),
            pl.BlockSpec((2, length, HD), lambda k: (0, 0, k)),
        ],
        out_specs=pl.BlockSpec((GROUP, 2, length), lambda k: (k, 0, 0)),
        out_shape=jax.ShapeDtypeStruct((heads, 2, length), jnp.float32),
        interpret=interpret,
    )(query_rows, keys_nat)


def map_from_gram(gram):
    eye = jnp.eye(gram.shape[0], dtype=gram.dtype)
    first = lax.linalg.triangular_solve(
        jnp.linalg.cholesky(gram), eye, left_side=False, lower=True, transpose_a=True
    )
    second_gram = highest(first.T, highest(gram, first))
    second = lax.linalg.triangular_solve(
        jnp.linalg.cholesky(second_gram), eye, left_side=False, lower=True, transpose_a=True
    )
    return highest(first, second)


def gram_of_pieces(pieces, r):
    full = lax.dot_general(pieces, pieces, (((0,), (0,)), ((), ())), preferred_element_type=jnp.float32)
    block = lambda a, b: full[a * r : (a + 1) * r, b * r : (b + 1) * r]
    order = [(1, 1), (0, 1), (1, 0), (0, 0)]
    total = block(*order[0])
    for a, b in order[1:]:
        total = total + block(a, b)
    return total


def apply_to_pieces(pieces, mapping, r):
    mh, mm, ml = split3(mapping)
    zero = jnp.zeros_like(mh)
    stack = jnp.concatenate(
        [
            jnp.concatenate([mh, mm, ml], axis=1),
            jnp.concatenate([mh, mm, zero], axis=1),
        ],
        axis=0,
    )
    out = jnp.dot(pieces, stack, preferred_element_type=jnp.float32)
    return (out[:, 2 * r :] + out[:, r : 2 * r]) + out[:, :r]


def split3(values):
    hi = lax.reduce_precision(values, exponent_bits=8, mantissa_bits=7)
    rest = values - hi
    mid = lax.reduce_precision(rest, exponent_bits=8, mantissa_bits=7)
    lo = rest - mid
    return [piece.astype(jnp.bfloat16) for piece in (hi, mid, lo)]


def total_over(values, axis):
    n = lax.axis_size(axis)
    spread = jnp.broadcast_to(values[None], (n,) + values.shape)
    return jnp.sum(lax.all_to_all(spread, axis, 0, 0, tiled=True), axis=0)


def local(tokens, queries, key_weight, u_factor, v_factor):
    n_seq = lax.axis_size("seq")
    me_seq = lax.axis_index("seq")
    me_fsdp = lax.axis_index("fsdp")
    slice_width = key_weight.shape[1]
    rows = u_factor.shape[0]

    packed = jnp.concatenate([key_weight] + split3(u_factor)[:2], axis=1)
    whole = lax.all_gather(packed, "fsdp", axis=0, tiled=True)

    x_local = tokens[0]
    chunk = x_local.shape[0]
    chunks = [x_local]
    for shift in range(1, n_seq):
        chunks.append(lax.ppermute(x_local, "seq", [(i, (i + shift) % n_seq) for i in range(n_seq)]))

    q_v = orthonormal(v_factor)
    weight_piece = whole[:, :slice_width]
    r = u_factor.shape[1]
    pieces = whole[:, slice_width:]
    q_u = apply_to_pieces(pieces, map_from_gram(gram_of_pieces(pieces, r)), r)
    q_low = q_u.astype(jnp.bfloat16)
    both = jnp.concatenate([weight_piece, q_low], axis=1)

    col_start = me_seq * slice_width
    v_slice = lax.dynamic_slice_in_dim(q_v, col_start, slice_width, 0)
    prod = jnp.dot(jnp.concatenate(chunks, axis=0), both, preferred_element_type=jnp.float32)
    base = prod[:, :slice_width]
    side = prod[:, slice_width:]
    offset = 2.0 * highest(side, v_slice.T)
    keys = jnp.stack([base + offset, base - offset]).astype(jnp.bfloat16)
    length = keys.shape[1]

    backwards = jnp.concatenate([keys[:, (n_seq - 1 - j) * chunk : (n_seq - j) * chunk] for j in range(n_seq)], axis=1)
    doubled = jnp.concatenate([backwards, backwards], axis=1)
    start = ((n_seq - 1 - me_seq) % n_seq) * chunk
    keys_nat = lax.dynamic_slice_in_dim(doubled, start, length, 1)
    partial_sums = jnp.sum(lse_rows(queries[0], keys_nat), axis=(0, 2))
    sums = total_over(total_over(partial_sums, "fsdp"), "seq")
    losses = sums / (lax.axis_size("fsdp") * length * HQ)
    unit = math.sqrt(D * KD / R)
    u_rows = lax.dynamic_slice_in_dim(q_u, me_fsdp * rows, rows, 0)
    update = unit * highest(u_rows, q_v.T)
    return (update, losses)


def solution(mesh):
    in_specs = (
        P("fsdp", "seq", None),
        P("fsdp", None, "seq"),
        P("fsdp", "seq"),
        P("fsdp", None),
        P(),
    )
    out_specs = (P("fsdp", None), P())
    return jax.shard_map(local, mesh=mesh, in_specs=in_specs, out_specs=out_specs, check_vma=False)
```

```python
import math

import jax
import jax.numpy as jnp
from jax import lax
from jax.experimental import pallas as pl
from jax.sharding import PartitionSpec as P
import functools

D = 8192
HQ = 64
HD = 128
R = 64
KD = 1024
GROUP = 8


def highest(left, right):
    return jnp.dot(left, right, precision=lax.Precision.HIGHEST, preferred_element_type=jnp.float32)


def solve_rows(rows, gram):
    lower = jnp.linalg.cholesky(gram)
    return lax.linalg.triangular_solve(lower, rows, left_side=False, lower=True, transpose_a=True)


def orthonormal(factor):
    for turn in range(2):
        factor = solve_rows(factor, highest(factor.T, factor))
    return factor


def orthonormal_map(factor):
    gram = highest(factor.T, factor)
    eye = jnp.eye(gram.shape[0], dtype=gram.dtype)
    first = lax.linalg.triangular_solve(
        jnp.linalg.cholesky(gram), eye, left_side=False, lower=True, transpose_a=True
    )
    second_gram = highest(first.T, highest(gram, first))
    second = lax.linalg.triangular_solve(
        jnp.linalg.cholesky(second_gram), eye, left_side=False, lower=True, transpose_a=True
    )
    return highest(factor, highest(first, second))


def lse_kernel(q_ref, k_ref, o_ref, *, blk, n_blk, scale):
    def one_head(g, carry):
        col = pl.multiple_of(g * HD, HD)
        for p in range(2):
            for qb in range(n_blk):
                q_blk = q_ref[qb * blk:(qb + 1) * blk, pl.ds(col, HD)]
                m = None
                l = None
                for kb in range(qb + 1):
                    k_blk = k_ref[p, kb * blk:(kb + 1) * blk, :]
                    s = lax.dot_general(k_blk, q_blk, (((1,), (1,)), ((), ())),
                                        preferred_element_type=jnp.float32) * scale
                    if kb == qb:
                        rows = lax.broadcasted_iota(jnp.int32, s.shape, 0)
                        cols = lax.broadcasted_iota(jnp.int32, s.shape, 1)
                        s = jnp.where(rows <= cols, s, -1e30)
                    top = jnp.max(s, axis=0, keepdims=True)
                    if m is None:
                        m = top
                        l = jnp.sum(jnp.exp(s - m), axis=0, keepdims=True)
                    else:
                        m_new = jnp.maximum(m, top)
                        l = l * jnp.exp(m - m_new) + jnp.sum(jnp.exp(s - m_new), axis=0, keepdims=True)
                        m = m_new
                o_ref[pl.ds(g, 1), p, qb * blk:(qb + 1) * blk] = (m + jnp.log(l))
        return carry

    lax.fori_loop(0, GROUP, one_head, 0)


def lse_rows(query_rows, keys_nat, interpret=False):
    length = query_rows.shape[0]
    heads = query_rows.shape[1] // HD
    kv = keys_nat.shape[2] // HD
    blk = 128
    kern = functools.partial(lse_kernel, blk=blk, n_blk=length // blk, scale=1.0 / math.sqrt(HD))
    return pl.pallas_call(
        kern,
        grid=(kv,),
        in_specs=[
            pl.BlockSpec((length, GROUP * HD), lambda k: (0, k)),
            pl.BlockSpec((2, length, HD), lambda k: (0, 0, k)),
        ],
        out_specs=pl.BlockSpec((GROUP, 2, length), lambda k: (k, 0, 0)),
        out_shape=jax.ShapeDtypeStruct((heads, 2, length), jnp.float32),
        interpret=interpret,
    )(query_rows, keys_nat)


def map_from_gram(gram):
    eye = jnp.eye(gram.shape[0], dtype=gram.dtype)
    first = lax.linalg.triangular_solve(
        jnp.linalg.cholesky(gram), eye, left_side=False, lower=True, transpose_a=True
    )
    second_gram = highest(first.T, highest(gram, first))
    second = lax.linalg.triangular_solve(
        jnp.linalg.cholesky(second_gram), eye, left_side=False, lower=True, transpose_a=True
    )
    return highest(first, second)


def gram_of_pieces(pieces, r):
    full = lax.dot_general(pieces, pieces, (((0,), (0,)), ((), ())), preferred_element_type=jnp.float32)
    block = lambda a, b: full[a * r : (a + 1) * r, b * r : (b + 1) * r]
    order = [(1, 1), (0, 1), (1, 0), (0, 0)]
    total = block(*order[0])
    for a, b in order[1:]:
        total = total + block(a, b)
    return total


def apply_to_pieces(pieces, mapping, r):
    mh, mm, ml = split3(mapping)
    zero = jnp.zeros_like(mh)
    stack = jnp.concatenate(
        [
            jnp.concatenate([mh, mm, ml], axis=1),
            jnp.concatenate([mh, mm, zero], axis=1),
        ],
        axis=0,
    )
    out = jnp.dot(pieces, stack, preferred_element_type=jnp.float32)
    return (out[:, 2 * r :] + out[:, r : 2 * r]) + out[:, :r]


def split3(values):
    hi = lax.reduce_precision(values, exponent_bits=8, mantissa_bits=7)
    rest = values - hi
    mid = lax.reduce_precision(rest, exponent_bits=8, mantissa_bits=7)
    lo = rest - mid
    return [piece.astype(jnp.bfloat16) for piece in (hi, mid, lo)]


def total_over(values, axis):
    n = lax.axis_size(axis)
    spread = jnp.broadcast_to(values[None], (n,) + values.shape)
    return jnp.sum(lax.all_to_all(spread, axis, 0, 0, tiled=True), axis=0)


def local(tokens, queries, key_weight, u_factor, v_factor):
    n_seq = lax.axis_size("seq")
    me_seq = lax.axis_index("seq")
    me_fsdp = lax.axis_index("fsdp")
    slice_width = key_weight.shape[1]
    rows = u_factor.shape[0]

    packed = jnp.concatenate([key_weight] + split3(u_factor)[:2], axis=1)
    whole = lax.all_gather(packed, "fsdp", axis=0, tiled=True)

    x_local = tokens[0]
    chunk = x_local.shape[0]
    chunks = [x_local]
    for shift in range(1, n_seq):
        chunks.append(lax.ppermute(x_local, "seq", [(i, (i + shift) % n_seq) for i in range(n_seq)]))

    q_v = orthonormal(v_factor)
    r = u_factor.shape[1]
    pieces = whole[:, slice_width:]
    q_u = apply_to_pieces(pieces, map_from_gram(gram_of_pieces(pieces, r)), r)
    q_low = q_u.astype(jnp.bfloat16)
    both = lax.dynamic_update_slice_in_dim(whole, q_low, slice_width, 1)

    col_start = me_seq * slice_width
    v_slice = lax.dynamic_slice_in_dim(q_v, col_start, slice_width, 0)
    prod = jnp.dot(jnp.concatenate(chunks, axis=0), both, preferred_element_type=jnp.float32)
    base = prod[:, :slice_width]
    side = prod[:, slice_width : slice_width + r]
    offset = 2.0 * highest(side, v_slice.T)
    keys = jnp.stack([base + offset, base - offset]).astype(jnp.bfloat16)
    length = keys.shape[1]

    backwards = jnp.concatenate([keys[:, (n_seq - 1 - j) * chunk : (n_seq - j) * chunk] for j in range(n_seq)], axis=1)
    doubled = jnp.concatenate([backwards, backwards], axis=1)
    start = ((n_seq - 1 - me_seq) % n_seq) * chunk
    keys_nat = lax.dynamic_slice_in_dim(doubled, start, length, 1)
    partial_sums = jnp.sum(lse_rows(queries[0], keys_nat), axis=(0, 2))
    sums = total_over(total_over(partial_sums, "fsdp"), "seq")
    losses = sums / (lax.axis_size("fsdp") * length * HQ)
    unit = math.sqrt(D * KD / R)
    u_rows = lax.dynamic_slice_in_dim(q_u, me_fsdp * rows, rows, 0)
    update = unit * highest(u_rows, q_v.T)
    return (update, losses)


def solution(mesh):
    in_specs = (
        P("fsdp", "seq", None),
        P("fsdp", None, "seq"),
        P("fsdp", "seq"),
        P("fsdp", None),
        P(),
    )
    out_specs = (P("fsdp", None), P())
    return jax.shard_map(local, mesh=mesh, in_specs=in_specs, out_specs=out_specs, check_vma=False)
```

```python
import math

import jax
import jax.numpy as jnp
from jax import lax
from jax.experimental import pallas as pl
from jax.sharding import PartitionSpec as P
import functools

D = 8192
HQ = 64
HD = 128
R = 64
KD = 1024
GROUP = 8


def highest(left, right):
    return jnp.dot(left, right, precision=lax.Precision.HIGHEST, preferred_element_type=jnp.float32)


def solve_rows(rows, gram):
    lower = jnp.linalg.cholesky(gram)
    return lax.linalg.triangular_solve(lower, rows, left_side=False, lower=True, transpose_a=True)


def orthonormal(factor):
    for turn in range(2):
        factor = solve_rows(factor, highest(factor.T, factor))
    return factor


def orthonormal_map(factor):
    gram = highest(factor.T, factor)
    eye = jnp.eye(gram.shape[0], dtype=gram.dtype)
    first = lax.linalg.triangular_solve(
        jnp.linalg.cholesky(gram), eye, left_side=False, lower=True, transpose_a=True
    )
    second_gram = highest(first.T, highest(gram, first))
    second = lax.linalg.triangular_solve(
        jnp.linalg.cholesky(second_gram), eye, left_side=False, lower=True, transpose_a=True
    )
    return highest(factor, highest(first, second))


def lse_kernel(q_ref, k_ref, o_ref, *, blk, n_blk, scale):
    def one_head(g, carry):
        col = pl.multiple_of(g * HD, HD)
        for p in range(2):
            for qb in range(n_blk):
                q_blk = q_ref[qb * blk:(qb + 1) * blk, pl.ds(col, HD)]
                m = None
                l = None
                for kb in range(qb + 1):
                    k_blk = k_ref[p, kb * blk:(kb + 1) * blk, :]
                    s = lax.dot_general(k_blk, q_blk, (((1,), (1,)), ((), ())),
                                        preferred_element_type=jnp.float32) * scale
                    if kb == qb:
                        rows = lax.broadcasted_iota(jnp.int32, s.shape, 0)
                        cols = lax.broadcasted_iota(jnp.int32, s.shape, 1)
                        s = jnp.where(rows <= cols, s, -1e30)
                    top = jnp.max(s, axis=0, keepdims=True)
                    if m is None:
                        m = top
                        l = jnp.sum(jnp.exp(s - m), axis=0, keepdims=True)
                    else:
                        m_new = jnp.maximum(m, top)
                        l = l * jnp.exp(m - m_new) + jnp.sum(jnp.exp(s - m_new), axis=0, keepdims=True)
                        m = m_new
                o_ref[pl.ds(g, 1), p, qb * blk:(qb + 1) * blk] = (m + jnp.log(l))
        return carry

    lax.fori_loop(0, GROUP, one_head, 0)


def lse_rows(query_rows, keys_nat, interpret=False):
    length = query_rows.shape[0]
    heads = query_rows.shape[1] // HD
    kv = keys_nat.shape[2] // HD
    blk = 128
    kern = functools.partial(lse_kernel, blk=blk, n_blk=length // blk, scale=1.0 / math.sqrt(HD))
    return pl.pallas_call(
        kern,
        grid=(kv,),
        in_specs=[
            pl.BlockSpec((length, GROUP * HD), lambda k: (0, k)),
            pl.BlockSpec((2, length, HD), lambda k: (0, 0, k)),
        ],
        out_specs=pl.BlockSpec((GROUP, 2, length), lambda k: (k, 0, 0)),
        out_shape=jax.ShapeDtypeStruct((heads, 2, length), jnp.float32),
        interpret=interpret,
    )(query_rows, keys_nat)


def map_from_gram(gram):
    eye = jnp.eye(gram.shape[0], dtype=gram.dtype)
    first = lax.linalg.triangular_solve(
        jnp.linalg.cholesky(gram), eye, left_side=False, lower=True, transpose_a=True
    )
    second_gram = highest(first.T, highest(gram, first))
    second = lax.linalg.triangular_solve(
        jnp.linalg.cholesky(second_gram), eye, left_side=False, lower=True, transpose_a=True
    )
    return highest(first, second)


def gram_of_pieces(pieces, r):
    full = lax.dot_general(pieces, pieces, (((0,), (0,)), ((), ())), preferred_element_type=jnp.float32)
    block = lambda a, b: full[a * r : (a + 1) * r, b * r : (b + 1) * r]
    order = [(1, 1), (0, 1), (1, 0), (0, 0)]
    total = block(*order[0])
    for a, b in order[1:]:
        total = total + block(a, b)
    return total


def apply_to_pieces(pieces, mapping, r):
    mh, mm, ml = split3(mapping)
    zero = jnp.zeros_like(mh)
    stack = jnp.concatenate(
        [
            jnp.concatenate([mh, mm, ml], axis=1),
            jnp.concatenate([mh, mm, zero], axis=1),
        ],
        axis=0,
    )
    out = jnp.dot(pieces, stack, preferred_element_type=jnp.float32)
    return (out[:, 2 * r :] + out[:, r : 2 * r]) + out[:, :r]


def split3(values):
    hi = lax.reduce_precision(values, exponent_bits=8, mantissa_bits=7)
    rest = values - hi
    mid = lax.reduce_precision(rest, exponent_bits=8, mantissa_bits=7)
    lo = rest - mid
    return [piece.astype(jnp.bfloat16) for piece in (hi, mid, lo)]


def total_over(values, axis):
    n = lax.axis_size(axis)
    spread = jnp.broadcast_to(values[None], (n,) + values.shape)
    return jnp.sum(lax.all_to_all(spread, axis, 0, 0, tiled=True), axis=0)


def local(tokens, queries, key_weight, u_factor, v_factor):
    n_seq = lax.axis_size("seq")
    me_seq = lax.axis_index("seq")
    me_fsdp = lax.axis_index("fsdp")
    slice_width = key_weight.shape[1]
    rows = u_factor.shape[0]

    packed = jnp.concatenate([key_weight] + split3(u_factor)[:2], axis=1)
    whole = lax.all_gather(packed, "fsdp", axis=0, tiled=True)

    x_local = tokens[0]
    chunk = x_local.shape[0]
    chunks = [x_local]
    for shift in range(1, n_seq):
        chunks.append(lax.ppermute(x_local, "seq", [(i, (i + shift) % n_seq) for i in range(n_seq)]))

    q_v = orthonormal(v_factor)
    r = u_factor.shape[1]
    pieces = whole[:, slice_width:]
    q_u = apply_to_pieces(pieces, map_from_gram(gram_of_pieces(pieces, r)), r)
    q_low = q_u.astype(jnp.bfloat16)

    col_start = me_seq * slice_width
    v_slice = lax.dynamic_slice_in_dim(q_v, col_start, slice_width, 0)
    x_all = jnp.concatenate(chunks, axis=0)
    base = jnp.dot(x_all, whole, preferred_element_type=jnp.float32)[:, :slice_width]
    side = jnp.dot(x_all, q_low, preferred_element_type=jnp.float32)
    offset = 2.0 * highest(side, v_slice.T)
    keys = jnp.stack([base + offset, base - offset]).astype(jnp.bfloat16)
    length = keys.shape[1]

    backwards = jnp.concatenate([keys[:, (n_seq - 1 - j) * chunk : (n_seq - j) * chunk] for j in range(n_seq)], axis=1)
    doubled = jnp.concatenate([backwards, backwards], axis=1)
    start = ((n_seq - 1 - me_seq) % n_seq) * chunk
    keys_nat = lax.dynamic_slice_in_dim(doubled, start, length, 1)
    partial_sums = jnp.sum(lse_rows(queries[0], keys_nat), axis=(0, 2))
    sums = total_over(total_over(partial_sums, "fsdp"), "seq")
    losses = sums / (lax.axis_size("fsdp") * length * HQ)
    unit = math.sqrt(D * KD / R)
    u_rows = lax.dynamic_slice_in_dim(q_u, me_fsdp * rows, rows, 0)
    update = unit * highest(u_rows, q_v.T)
    return (update, losses)


def solution(mesh):
    in_specs = (
        P("fsdp", "seq", None),
        P("fsdp", None, "seq"),
        P("fsdp", "seq"),
        P("fsdp", None),
        P(),
    )
    out_specs = (P("fsdp", None), P())
    return jax.shard_map(local, mesh=mesh, in_specs=in_specs, out_specs=out_specs, check_vma=False)
```
